1024 devices in a mesh: tile: 64 (over x, y, core), chan: 16 (over z).
Axes of the slice: x: 4, y: 8, z: 16, core: 2. Of those that a mesh axis runs over, the one named last changes fastest.
Arguments:
- points: bfloat16 [128, 65536], P('chan', 'tile'), may hold values from -6 to 6
- dest: int32 [65536, 1], P('tile'), may hold values from 0 to 63; in each aligned block of 1024 rows (0 to 1023, 1024 to 2047, ...) at most 48 rows name the same one
- voxel: int32 [65536, 1], P('tile'), may hold values from 0 to 2047
- weight: bfloat16 [256, 27, 128], P('chan'), may hold values from -0.109375 to 0.109375
- grad_out: bfloat16 [256, 131072], P('chan', 'tile'), may hold values from -6 to 6
Outputs:
- features_out: bfloat16 [256, 131072], P('chan', 'tile')
- weight_grad: float32 [256, 3456], P('chan', 'tile')
The draws below stay inside these ranges and needn't reach their ends.
Inputs may be any that keep to these rules, and one draw needn't show every extreme that they name: `dest`: among the 1024 points of one scene owner (aligned blocks of rows), at most 48 go to any one tile, and some tile receives exactly 48 of them.
All inputs are finite; a program needn't handle non-finite values.
Results may differ from the reference program's by a relative error of at most 0.0029.
Values may be sent and summed in bfloat16 or wider, within the bound.
No kernel may reach another device: no remote copies, remote signals or barrier semaphores. Data moves between devices by JAX's collectives and lax.ppermute only.
A program may use at most 64 MiB of HBM per device.

```python
import math
import jax
import jax.numpy as jnp
import numpy as np
from jax import lax

C_IN = 128
C_OUT = 256
EDGE = 16
DEPTH = 8
PTS_DEV = 1024
VOX = 2048
TILES = 64
POINTS = 65536
CAP = 48


def place_ends(values, own_key, low, largest):
    spot = [jax.random.randint(jax.random.fold_in(own_key, axis), (), 0, length) for axis, length in enumerate(values.shape)]
    widest = values.shape.index(max(values.shape))
    neighbour = spot[:widest] + [(spot[widest] + 1) % values.shape[widest]] + spot[widest + 1:]
    return values.at[tuple(spot)].set(low).at[tuple(neighbour)].set(largest)


def block_scale(stream_key, shape, pieces, smallest, high):
    level, own = 1.0, jax.random.fold_in(stream_key, 6)
    for dim, shards_of in pieces:
        steps = jnp.exp(jax.random.uniform(jax.random.fold_in(own, dim), (shards_of,), jnp.float32, smallest / len(pieces), high / len(pieces)))
        level = level * jnp.repeat(steps, shape[dim] // shards_of).reshape([-1 if axis == dim else 1 for axis in range(len(shape))])
    return level


def shared_out(key, own, number, rows, amount, top, limit, lean):
    sequence = jax.random.permutation(key, amount)
    packed, common = portions_of(amount, rows * top, limit, lean, True), portions_of(amount, rows * top, limit, lean, False)
    places = jnp.arange(amount)

    def named(lengths, rotation):
        used = int((lengths > 0).sum())
        fixed = max(1, used // 4)
        shifted = fixed + (places - fixed + rotation * (used - fixed)) % max(1, amount - fixed)
        return jnp.zeros((amount,), jnp.int32).at[sequence[jnp.where(places < fixed, places, shifted)]].set(jnp.asarray(lengths, jnp.int32))

    lengths = jnp.where(number % 4 == 0, named(packed, number // 4), named(common, number - number // 4 - 1))
    mixed = jax.random.permutation(jax.random.fold_in(own, 3), amount)
    donor, taker = mixed[0:amount // 2 * 2:2], mixed[1:amount // 2 * 2:2]
    slack = jnp.minimum(lengths[donor] - 1, limit - lengths[taker]) // 2
    slack = jnp.where((donor == sequence[0]) | (taker == sequence[0]) | (lengths[taker] == 0), 0, jnp.maximum(slack, 0))
    shifted = jax.random.randint(jax.random.fold_in(own, 4), (amount // 2,), 0, 1 << 20) % (slack + 1)
    lengths = lengths.at[donor].add(-shifted).at[taker].add(shifted)
    items = jnp.searchsorted(jnp.cumsum(lengths), jnp.arange(rows * top), side="right").astype(jnp.int32)
    table = items.reshape(top, rows).T
    table = table[jax.random.permutation(jax.random.fold_in(own, 1), rows)]
    rotation = jax.random.randint(jax.random.fold_in(own, 2), (rows, 1), 0, top)
    return jnp.take_along_axis(table, (jnp.arange(top)[None, :] + rotation) % top, axis=1)


def portions_of(count, total, limit, lean, full):
    weights = [(1 << 20) // math.isqrt(rank ** lean) + 1 for rank in range(1, count + 1)]
    largest = limit if full else min(limit, max(-(-total // count), total * weights[0] // sum(weights)))
    least = 1 if total - largest >= count - 1 else 0
    given, rest = [largest] + [least] * (count - 1), total - largest - least * (count - 1)
    while rest > 0:
        free = [i for i in range(1, count) if given[i] < largest] or [i for i in range(1, count) if given[i] < limit]
        pool, remaining = sum([weights[i] for i in free]), rest
        for i in free:
            addition = min(limit - given[i], max(1, remaining * weights[i] // pool), rest)
            given[i] = given[i] + addition
            rest = rest - addition
    return np.array(given)


def bell_draw(rng, extent, scale, most, shards=(), held_as=jnp.bfloat16):
    entries = scale * jax.random.normal(rng, extent, jnp.float32)
    if shards:
        entries = entries * block_scale(rng, extent, shards, -0.22, 0.18)
    return jnp.clip(entries, -most, most).astype(held_as)


def setup_inputs(seed: int = 0) -> dict:
    streams_of = jax.random.split(jax.random.key(seed), 6)
    points = bell_draw(streams_of[0], (C_IN, POINTS), 1.0, 6.0, ((0, 16), (1, 64)))
    dest_keys = jax.random.split(jax.random.fold_in(streams_of[1], 1), POINTS // PTS_DEV)
    dest_turns = jax.random.permutation(jax.random.fold_in(streams_of[1], 3), POINTS // PTS_DEV)
    dest = jax.vmap(lambda own, number: shared_out(jax.random.fold_in(streams_of[1], 2), own, number, PTS_DEV, TILES, 1, CAP, 2))(dest_keys, dest_turns).reshape((POINTS, 1))
    voxel = place_ends(jax.random.randint(streams_of[2], (POINTS, 1), 0, VOX), jax.random.fold_in(streams_of[2], 1), 0, VOX - 1).astype(jnp.int32)
    weight = bell_draw(streams_of[3], (C_OUT, 27, C_IN), (27 * C_IN) ** -0.5, 0.109375, ((0, 16),))
    grad_out = bell_draw(streams_of[4], (C_OUT, TILES * VOX), 1.0, 6.0, ((0, 16), (1, 64)))
    return {"points": points, "dest": dest, "voxel": voxel, "weight": weight, "grad_out": grad_out}


def tile_conv(grid_part, weight_part, masked):
    count = grid_part.shape[0]
    cube = grid_part.reshape(count, DEPTH, EDGE, EDGE)
    padded = jnp.pad(cube, ((0, 0), (1, 1), (1, 1), (1, 1)))
    output = jnp.zeros((weight_part.shape[0], DEPTH * EDGE * EDGE), jnp.float32)
    grads = []
    for index in range(27):
        first, second, third = index // 9, (index // 3) % 3, index % 3
        moved = padded[:, first:first + DEPTH, second:second + EDGE, third:third + EDGE].reshape(count, DEPTH * EDGE * EDGE)
        output = output + jnp.dot(weight_part[:, index, :], moved, preferred_element_type=jnp.float32)
        grads.append(lax.dot_general(masked, moved, (((1,), (1,)), ((), ())), preferred_element_type=jnp.float32))
    return output, jnp.stack(grads, axis=1)


def reference(points, dest, voxel, weight, grad_out):
    cell = dest[:, 0].astype(jnp.int32) * VOX + voxel[:, 0].astype(jnp.int32)
    sums = jax.ops.segment_sum(points.astype(jnp.float32).T, cell, num_segments=TILES * VOX)
    counts = jax.ops.segment_sum(jnp.ones(cell.shape, jnp.float32), cell, num_segments=TILES * VOX)
    grid = (sums / jnp.maximum(counts, 1.0)[:, None]).astype(jnp.bfloat16)
    grid = grid.reshape(TILES, VOX, C_IN).transpose(0, 2, 1)
    occupied = (counts > 0).astype(jnp.float32).reshape(TILES, VOX)
    cotangent = grad_out.reshape(C_OUT, TILES, VOX).transpose(1, 0, 2)

    def one_tile(total, items):
        grid_tile, mask_tile, cot_tile = items
        masked = (cot_tile.astype(jnp.float32) * mask_tile[None, :]).astype(jnp.bfloat16)
        output, grads = tile_conv(grid_tile, weight, masked)
        return total + grads, (output * mask_tile[None, :]).astype(jnp.bfloat16)

    total, outputs = lax.scan(one_tile, jnp.zeros((C_OUT, 27, C_IN), jnp.float32), (grid, occupied, cotangent))
    features_out = outputs.transpose(1, 0, 2).reshape(C_OUT, TILES * VOX)
    return features_out, total.reshape(C_OUT, 27 * C_IN)
```

```python
import jax
import jax.numpy as jnp
import numpy as np
from jax import lax
from jax.sharding import Mesh
from jax.sharding import PartitionSpec as P

C_IN = 128
EDGE = 16
DEPTH = 8
VOX = 2048
OFFSETS = [(k // 9 - 1, k // 3 % 3 - 1, k % 3 - 1) for k in range(27)]
TILE_AXES = ("tx", "ty", "tc")


def shift_sum(y, signs):
    count = y.shape[1]
    cube = y.reshape(27, count, DEPTH, EDGE, EDGE)
    padded = jnp.pad(cube, ((0, 0), (0, 0), (1, 1), (1, 1), (1, 1)))
    total = None
    for k, (a, b, e) in enumerate(OFFSETS):
        a, b, e = signs * a + 1, signs * b + 1, signs * e + 1
        part = padded[k, :, a : a + DEPTH, b : b + EDGE, e : e + EDGE]
        total = part if total is None else total + part
    return total.reshape(count, VOX)


def shifted_stack(x, signs):
    count = x.shape[0]
    cube = x.reshape(count, DEPTH, EDGE, EDGE)
    padded = jnp.pad(cube, ((0, 0), (1, 1), (1, 1), (1, 1)))
    parts = []
    for a, b, e in OFFSETS:
        a, b, e = signs * a + 1, signs * b + 1, signs * e + 1
        parts.append(padded[:, a : a + DEPTH, b : b + EDGE, e : e + EDGE].reshape(count, VOX))
    return jnp.concatenate(parts, axis=0)


def on_device(tiles, points, dest, voxel, weight, grad_out):
    count = dest.shape[0]
    capacity = min(count, 3 * count // tiles)
    slots = tiles * capacity
    out_rows = weight.shape[0]
    channels = points.shape[0]

    onehot = (dest == jnp.arange(tiles, dtype=jnp.int32)[None, :]).astype(jnp.bfloat16)
    rows = jnp.arange(count, dtype=jnp.int32)
    earlier = (rows[:, None] > rows[None, :]).astype(jnp.bfloat16)
    before = jnp.dot(earlier, onehot, preferred_element_type=jnp.float32)
    rank = jnp.sum(before * onehot.astype(jnp.float32), axis=1).astype(jnp.int32)
    place = dest[:, 0] * capacity + rank

    vox = voxel[:, 0]
    codes = jnp.stack([vox // 64 + 1, vox % 64]).astype(jnp.bfloat16)
    payload = jnp.concatenate([points, codes], axis=0)
    select = (place[:, None] == jnp.arange(slots, dtype=jnp.int32)[None, :]).astype(jnp.bfloat16)
    send = jnp.dot(payload, select, preferred_element_type=jnp.float32).astype(jnp.bfloat16)
    received = lax.all_to_all(send, TILE_AXES, split_axis=1, concat_axis=1, tiled=True)

    high = received[channels].astype(jnp.int32)
    low = received[channels + 1].astype(jnp.int32)
    cell = jnp.where(high > 0, (high - 1) * 64 + low, VOX)
    member = (cell[:, None] == jnp.arange(VOX, dtype=jnp.int32)[None, :]).astype(jnp.bfloat16)
    summed = jnp.concatenate(
        [received[:channels], jnp.ones((1, slots), jnp.bfloat16)], axis=0
    )
    sums = jnp.dot(summed, member, preferred_element_type=jnp.float32)
    counts = sums[channels]
    grid = (sums[:channels] / jnp.maximum(counts, 1.0)[None, :]).astype(jnp.bfloat16)
    occupied = (counts > 0).astype(jnp.float32)

    full = lax.all_gather(grid, "chan", axis=0, tiled=True)
    masked = (grad_out.astype(jnp.float32) * occupied[None, :]).astype(jnp.bfloat16)

    stacked_w = weight.transpose(1, 0, 2).reshape(27 * out_rows, C_IN)
    partial = jnp.dot(stacked_w, full, preferred_element_type=jnp.float32)
    output = shift_sum(partial.reshape(27, out_rows, VOX), 1)
    features_out = (output * occupied[None, :]).astype(jnp.bfloat16)

    moved = shifted_stack(masked, -1)
    grads = lax.dot_general(
        moved, full, (((1,), (1,)), ((), ())), preferred_element_type=jnp.float32
    )
    grads = grads.reshape(27, out_rows, C_IN).transpose(1, 0, 2).reshape(out_rows, 27 * C_IN)
    width = grads.shape[1] // tiles
    chunks = grads.reshape(out_rows, tiles, width).transpose(1, 0, 2)
    weight_grad = lax.psum_scatter(chunks, TILE_AXES, scatter_dimension=0, tiled=True)
    return (features_out, weight_grad.reshape(out_rows, width))


def solution(mesh):
    tiles, chans = mesh.devices.shape
    split = Mesh(mesh.devices.reshape(4, tiles // 8, 2, chans), (*TILE_AXES, "chan"))
    tile = TILE_AXES
    placed = (
        P("chan", tile),
        P(tile, None),
        P(tile, None),
        P("chan", None, None),
        P("chan", tile),
    )

    def step(*args):
        return on_device(tiles, *args)

    return jax.shard_map(
        step,
        mesh=split,
        in_specs=placed,
        out_specs=(P("chan", tile), P("chan", tile)),
        check_vma=False,
    )
```

```python
import jax
import jax.numpy as jnp
import numpy as np
from jax import lax
from jax.sharding import Mesh
from jax.sharding import PartitionSpec as P

C_IN = 128
EDGE = 16
DEPTH = 8
VOX = 2048
OFFSETS = [(k // 9 - 1, k // 3 % 3 - 1, k % 3 - 1) for k in range(27)]
TILE_AXES = ("tx", "ty", "tc")


REACH = 256 + 16 + 1


def valid(a, b, e):
    v = lax.broadcasted_iota(jnp.int32, (1, VOX), 1)
    i, j, l = v // (EDGE * EDGE), v // EDGE % EDGE, v % EDGE
    return (
        (i + a >= 0) & (i + a < DEPTH) & (j + b >= 0) & (j + b < EDGE) & (l + e >= 0) & (l + e < EDGE)
    )


def shifted(padded, k, signs):
    a, b, e = (signs * x for x in OFFSETS[k])
    d = (a * EDGE + b) * EDGE + e
    part = padded[:, REACH + d : REACH + d + VOX]
    return jnp.where(valid(a, b, e), part, jnp.zeros_like(part))


def on_device(tiles, points, dest, voxel, weight, grad_out):
    count = dest.shape[0]
    capacity = min(count, 3 * count // tiles)
    slots = tiles * capacity
    out_rows = weight.shape[0]
    channels = points.shape[0]

    onehot = (dest == jnp.arange(tiles, dtype=jnp.int32)[None, :]).astype(jnp.bfloat16)
    rows = jnp.arange(count, dtype=jnp.int32)
    earlier = (rows[:, None] > rows[None, :]).astype(jnp.bfloat16)
    before = jnp.dot(earlier, onehot, preferred_element_type=jnp.float32)
    rank = jnp.sum(before * onehot.astype(jnp.float32), axis=1).astype(jnp.int32)
    place = dest[:, 0] * capacity + rank

    vox = voxel[:, 0]
    codes = jnp.stack([vox // 64 + 1, vox % 64]).astype(jnp.bfloat16)
    payload = jnp.concatenate([points, codes], axis=0)
    select = (place[:, None] == jnp.arange(slots, dtype=jnp.int32)[None, :]).astype(jnp.bfloat16)
    send = jnp.dot(payload, select, preferred_element_type=jnp.float32).astype(jnp.bfloat16)
    received = lax.all_to_all(send, TILE_AXES, split_axis=1, concat_axis=1, tiled=True)

    high = received[channels].astype(jnp.int32)
    low = received[channels + 1].astype(jnp.int32)
    cell = jnp.where(high > 0, (high - 1) * 64 + low, VOX)
    member = (cell[:, None] == jnp.arange(VOX, dtype=jnp.int32)[None, :]).astype(jnp.bfloat16)
    summed = jnp.concatenate(
        [received[:channels], jnp.ones((1, slots), jnp.bfloat16)], axis=0
    )
    sums = jnp.dot(summed, member, preferred_element_type=jnp.float32)
    counts = sums[channels]
    grid = (sums[:channels] / jnp.maximum(counts, 1.0)[None, :]).astype(jnp.bfloat16)
    occupied = (counts > 0).astype(jnp.float32)

    full = lax.all_gather(grid, "chan", axis=0, tiled=True)
    masked = (grad_out.astype(jnp.float32) * occupied[None, :]).astype(jnp.bfloat16)

    stacked_w = weight.transpose(1, 0, 2).reshape(27 * out_rows, C_IN)
    wide = jnp.pad(full, ((0, 0), (REACH, REACH)))
    partial = jnp.dot(stacked_w, wide, preferred_element_type=jnp.float32)
    output = None
    for k in range(27):
        part = shifted(partial[k * out_rows : (k + 1) * out_rows], k, 1)
        output = part if output is None else output + part
    features_out = (output * occupied[None, :]).astype(jnp.bfloat16)

    wide_masked = jnp.pad(masked, ((0, 0), (REACH, REACH)))
    moved = jnp.stack([shifted(wide_masked, k, -1) for k in range(27)]).reshape(27 * out_rows, VOX)
    grads = lax.dot_general(
        moved, full, (((1,), (1,)), ((), ())), preferred_element_type=jnp.float32
    )
    grads = grads.reshape(27, out_rows, C_IN).transpose(1, 0, 2).reshape(out_rows, 27 * C_IN)
    width = grads.shape[1] // tiles
    chunks = grads.reshape(out_rows, tiles, width).transpose(1, 0, 2)
    arrived = lax.all_to_all(chunks, TILE_AXES, split_axis=0, concat_axis=0, tiled=True)
    weight_grad = jnp.sum(arrived, axis=0)
    return (features_out, weight_grad)


def solution(mesh):
    tiles, chans = mesh.devices.shape
    split = Mesh(mesh.devices.reshape(4, tiles // 8, 2, chans), (*TILE_AXES, "chan"))
    tile = TILE_AXES
    placed = (
        P("chan", tile),
        P(tile, None),
        P(tile, None),
        P("chan", None, None),
        P("chan", tile),
    )

    def step(*args):
        return on_device(tiles, *args)

    return jax.shard_map(
        step,
        mesh=split,
        in_specs=placed,
        out_specs=(P("chan", tile), P("chan", tile)),
        check_vma=False,
    )
```

```python
import jax
import jax.numpy as jnp
import numpy as np
from jax import lax
from jax.sharding import Mesh
from jax.sharding import PartitionSpec as P

C_IN = 128
EDGE = 16
DEPTH = 8
VOX = 2048
OFFSETS = [(k // 9 - 1, k // 3 % 3 - 1, k % 3 - 1) for k in range(27)]
TILE_AXES = ("tx", "ty", "tc")


REACH = 256 + 16 + 1


def valid(a, b, e):
    v = lax.broadcasted_iota(jnp.int32, (1, VOX), 1)
    i, j, l = v // (EDGE * EDGE), v // EDGE % EDGE, v % EDGE
    return (
        (i + a >= 0) & (i + a < DEPTH) & (j + b >= 0) & (j + b < EDGE) & (l + e >= 0) & (l + e < EDGE)
    )


def shifted(padded, k, signs):
    a, b, e = (signs * x for x in OFFSETS[k])
    d = (a * EDGE + b) * EDGE + e
    part = padded[:, REACH + d : REACH + d + VOX]
    return jnp.where(valid(a, b, e), part, jnp.zeros_like(part))


def on_device(tiles, points, dest, voxel, weight, grad_out):
    count = dest.shape[0]
    capacity = min(count, 3 * count // tiles)
    slots = tiles * capacity
    out_rows = weight.shape[0]
    channels = points.shape[0]

    onehot = (dest == jnp.arange(tiles, dtype=jnp.int32)[None, :]).astype(jnp.bfloat16)
    rows = jnp.arange(count, dtype=jnp.int32)
    earlier = (rows[:, None] > rows[None, :]).astype(jnp.bfloat16)
    before = jnp.dot(earlier, onehot, preferred_element_type=jnp.float32)
    rank = jnp.sum(before * onehot.astype(jnp.float32), axis=1).astype(jnp.int32)
    place = dest[:, 0] * capacity + rank

    vox = voxel[:, 0]
    codes = jnp.stack([vox // 64 + 1, vox % 64]).astype(jnp.bfloat16)
    payload = jnp.concatenate([points, codes], axis=0)
    select = (place[:, None] == jnp.arange(slots, dtype=jnp.int32)[None, :]).astype(jnp.bfloat16)
    send = jnp.dot(payload, select, preferred_element_type=jnp.float32).astype(jnp.bfloat16)
    received = lax.all_to_all(send, TILE_AXES, split_axis=1, concat_axis=1, tiled=True)

    high = received[channels].astype(jnp.int32)
    low = received[channels + 1].astype(jnp.int32)
    cell = jnp.where(high > 0, (high - 1) * 64 + low, VOX)
    member = (cell[:, None] == jnp.arange(VOX, dtype=jnp.int32)[None, :]).astype(jnp.bfloat16)
    summed = jnp.concatenate(
        [received[:channels], jnp.ones((1, slots), jnp.bfloat16)], axis=0
    )
    sums = jnp.dot(summed, member, preferred_element_type=jnp.float32)
    counts = sums[channels]
    grid = (sums[:channels] / jnp.maximum(counts, 1.0)[None, :]).astype(jnp.bfloat16)
    occupied = (counts > 0).astype(jnp.float32)

    chans = lax.axis_size("chan")
    copies = jnp.broadcast_to(grid[None], (chans, *grid.shape))
    full = lax.all_to_all(copies, "chan", split_axis=0, concat_axis=0, tiled=True)
    full = full.reshape(chans * channels, VOX)
    masked = (grad_out.astype(jnp.float32) * occupied[None, :]).astype(jnp.bfloat16)

    stacked_w = weight.transpose(1, 0, 2).reshape(27 * out_rows, C_IN)
    wide = jnp.pad(full, ((0, 0), (REACH, REACH)))
    partial = jnp.dot(stacked_w, wide, preferred_element_type=jnp.float32)
    output = None
    for k in range(27):
        part = shifted(partial[k * out_rows : (k + 1) * out_rows], k, 1)
        output = part if output is None else output + part
    features_out = (output * occupied[None, :]).astype(jnp.bfloat16)

    wide_masked = jnp.pad(masked, ((0, 0), (REACH, REACH)))
    moved = jnp.stack([shifted(wide_masked, k, -1) for k in range(27)]).reshape(27 * out_rows, VOX)
    grads = lax.dot_general(
        moved, full, (((1,), (1,)), ((), ())), preferred_element_type=jnp.float32
    )
    grads = grads.reshape(27, out_rows, C_IN).transpose(1, 0, 2).reshape(out_rows, 27 * C_IN)
    width = grads.shape[1] // tiles
    chunks = grads.reshape(out_rows, tiles, width).transpose(1, 0, 2)
    arrived = lax.all_to_all(chunks, TILE_AXES, split_axis=0, concat_axis=0, tiled=True)
    weight_grad = jnp.sum(arrived, axis=0)
    return (features_out, weight_grad)


def solution(mesh):
    tiles, chans = mesh.devices.shape
    split = Mesh(mesh.devices.reshape(4, tiles // 8, 2, chans), (*TILE_AXES, "chan"))
    tile = TILE_AXES
    placed = (
        P("chan", tile),
        P(tile, None),
        P(tile, None),
        P("chan", None, None),
        P("chan", tile),
    )

    def step(*args):
        return on_device(tiles, *args)

    return jax.shard_map(
        step,
        mesh=split,
        in_specs=placed,
        out_specs=(P("chan", tile), P("chan", tile)),
        check_vma=False,
    )
```

```python
import jax
import jax.numpy as jnp
import numpy as np
from jax import lax
from jax.sharding import Mesh
from jax.sharding import PartitionSpec as P

C_IN = 128
EDGE = 16
DEPTH = 8
VOX = 2048
OFFSETS = [(k // 9 - 1, k // 3 % 3 - 1, k % 3 - 1) for k in range(27)]
TILE_AXES = ("tx", "ty", "tc")


REACH = 256 + 16 + 1


def valid(a, b, e):
    v = lax.broadcasted_iota(jnp.int32, (1, VOX), 1)
    i, j, l = v // (EDGE * EDGE), v // EDGE % EDGE, v % EDGE
    return (
        (i + a >= 0) & (i + a < DEPTH) & (j + b >= 0) & (j + b < EDGE) & (l + e >= 0) & (l + e < EDGE)
    )


def shifted(padded, k, signs):
    a, b, e = (signs * x for x in OFFSETS[k])
    d = (a * EDGE + b) * EDGE + e
    part = padded[:, REACH + d : REACH + d + VOX]
    return jnp.where(valid(a, b, e), part, jnp.zeros_like(part))


def on_device(tiles, points, dest, voxel, weight, grad_out):
    count = dest.shape[0]
    capacity = min(count, 3 * count // tiles)
    slots = tiles * capacity
    out_rows = weight.shape[0]
    channels = points.shape[0]

    onehot = (dest == jnp.arange(tiles, dtype=jnp.int32)[None, :]).astype(jnp.bfloat16)
    rows = jnp.arange(count, dtype=jnp.int32)
    earlier = (rows[:, None] > rows[None, :]).astype(jnp.bfloat16)
    before = jnp.dot(earlier, onehot, preferred_element_type=jnp.float32)
    rank = jnp.sum(before * onehot.astype(jnp.float32), axis=1).astype(jnp.int32)
    place = dest[:, 0] * capacity + rank

    vox = voxel[:, 0]
    codes = jnp.stack([vox // 64 + 1, vox % 64]).astype(jnp.bfloat16)
    payload = jnp.concatenate([points, codes], axis=0)
    select = (place[:, None] == jnp.arange(slots, dtype=jnp.int32)[None, :]).astype(jnp.bfloat16)
    send = jnp.dot(payload, select, preferred_element_type=jnp.float32).astype(jnp.bfloat16)
    received = lax.all_to_all(send, TILE_AXES, split_axis=1, concat_axis=1, tiled=True)

    high = received[channels].astype(jnp.int32)
    low = received[channels + 1].astype(jnp.int32)
    cell = jnp.where(high > 0, (high - 1) * 64 + low, VOX)
    member = (cell[:, None] == jnp.arange(VOX, dtype=jnp.int32)[None, :]).astype(jnp.bfloat16)
    summed = jnp.concatenate(
        [received[:channels], jnp.ones((1, slots), jnp.bfloat16)], axis=0
    )
    sums = jnp.dot(summed, member, preferred_element_type=jnp.float32)
    counts = sums[channels]
    grid = (sums[:channels] / jnp.maximum(counts, 1.0)[None, :]).astype(jnp.bfloat16)
    occupied = (counts > 0).astype(jnp.float32)

    full = lax.all_gather(grid, "chan", axis=0, tiled=True)
    masked = (grad_out.astype(jnp.float32) * occupied[None, :]).astype(jnp.bfloat16)

    stacked_w = weight.transpose(1, 0, 2).reshape(27 * out_rows, C_IN)
    wide = jnp.pad(full, ((0, 0), (REACH, REACH)))
    partial = jnp.dot(stacked_w, wide, preferred_element_type=jnp.float32)
    output = None
    for k in range(27):
        part = shifted(partial[k * out_rows : (k + 1) * out_rows], k, 1)
        output = part if output is None else output + part
    features_out = (output * occupied[None, :]).astype(jnp.bfloat16)

    wide_masked = jnp.pad(masked, ((0, 0), (REACH, REACH)))
    moved = jnp.stack([shifted(wide_masked, k, -1) for k in range(27)])
    grads = lax.dot_general(
        moved.reshape(27 * out_rows, VOX), full, (((1,), (1,)), ((), ())),
        preferred_element_type=jnp.float32,
    )
    width = 27 * C_IN // tiles
    grads = grads.reshape(27, out_rows, C_IN).transpose(1, 0, 2).reshape(out_rows, tiles, width)
    chunks = grads.transpose(1, 0, 2).reshape(tiles, out_rows * width)
    arrived = lax.all_to_all(chunks, TILE_AXES, split_axis=0, concat_axis=0, tiled=True)
    weight_grad = jnp.sum(arrived, axis=0).reshape(out_rows, width)
    return (features_out, weight_grad)


def solution(mesh):
    tiles, chans = mesh.devices.shape
    split = Mesh(mesh.devices.reshape(4, tiles // 8, 2, chans), (*TILE_AXES, "chan"))
    tile = TILE_AXES
    placed = (
        P("chan", tile),
        P(tile, None),
        P(tile, None),
        P("chan", None, None),
        P("chan", tile),
    )

    def step(*args):
        return on_device(tiles, *args)

    return jax.shard_map(
        step,
        mesh=split,
        in_specs=placed,
        out_specs=(P("chan", tile), P("chan", tile)),
        check_vma=False,
    )
```

```python
import jax
import jax.numpy as jnp
import numpy as np
from jax import lax
from jax.sharding import Mesh
from jax.sharding import PartitionSpec as P

C_IN = 128
EDGE = 16
DEPTH = 8
VOX = 2048
OFFSETS = [(k // 9 - 1, k // 3 % 3 - 1, k % 3 - 1) for k in range(27)]
TILE_AXES = ("tx", "ty", "tc")


REACH = 256 + 16 + 1


def valid(a, b, e):
    v = lax.broadcasted_iota(jnp.int32, (1, VOX), 1)
    i, j, l = v // (EDGE * EDGE), v // EDGE % EDGE, v % EDGE
    return (
        (i + a >= 0) & (i + a < DEPTH) & (j + b >= 0) & (j + b < EDGE) & (l + e >= 0) & (l + e < EDGE)
    )


def shifted(padded, k, signs):
    a, b, e = (signs * x for x in OFFSETS[k])
    d = (a * EDGE + b) * EDGE + e
    part = padded[:, REACH + d : REACH + d + VOX]
    return jnp.where(valid(a, b, e), part, jnp.zeros_like(part))


def moved_stack(masked):
    v = lax.broadcasted_iota(jnp.int32, (1, VOX), 1)
    coords = (v // (EDGE * EDGE), v // EDGE % EDGE, v % EDGE)
    sizes = (DEPTH, EDGE, EDGE)
    strides = (EDGE * EDGE, EDGE, 1)
    stage = masked
    for axis in (2, 1, 0):
        step, size, where_ = strides[axis], sizes[axis], coords[axis]
        pads = [(0, 0)] * (stage.ndim - 1) + [(step, step)]
        wide = jnp.pad(stage, pads)
        parts = []
        for shift in (-1, 0, 1):
            part = wide[..., step - shift * step : step - shift * step + VOX]
            keep = (where_ - shift >= 0) & (where_ - shift < size)
            parts.append(jnp.where(keep, part, jnp.zeros_like(part)))
        stage = jnp.stack(parts)
    return stage.reshape(27 * masked.shape[0], VOX)


def on_device(tiles, points, dest, voxel, weight, grad_out):
    count = dest.shape[0]
    capacity = min(count, 3 * count // tiles)
    slots = tiles * capacity
    out_rows = weight.shape[0]
    channels = points.shape[0]

    onehot = (dest == jnp.arange(tiles, dtype=jnp.int32)[None, :]).astype(jnp.bfloat16)
    rows = jnp.arange(count, dtype=jnp.int32)
    earlier = (rows[:, None] > rows[None, :]).astype(jnp.bfloat16)
    before = jnp.dot(earlier, onehot, preferred_element_type=jnp.float32)
    rank = jnp.sum(before * onehot.astype(jnp.float32), axis=1).astype(jnp.int32)
    place = dest[:, 0] * capacity + rank

    vox = voxel[:, 0]
    codes = jnp.stack([vox // 64 + 1, vox % 64]).astype(jnp.bfloat16)
    payload = jnp.concatenate([points, codes], axis=0)
    select = (place[:, None] == jnp.arange(slots, dtype=jnp.int32)[None, :]).astype(jnp.bfloat16)
    send = jnp.dot(payload, select, preferred_element_type=jnp.float32).astype(jnp.bfloat16)
    received = lax.all_to_all(send, TILE_AXES, split_axis=1, concat_axis=1, tiled=True)

    high = received[channels].astype(jnp.int32)
    low = received[channels + 1].astype(jnp.int32)
    cell = jnp.where(high > 0, (high - 1) * 64 + low, VOX)
    member = (cell[:, None] == jnp.arange(VOX, dtype=jnp.int32)[None, :]).astype(jnp.bfloat16)
    summed = jnp.concatenate(
        [received[:channels], jnp.ones((1, slots), jnp.bfloat16)], axis=0
    )
    sums = jnp.dot(summed, member, preferred_element_type=jnp.float32)
    counts = sums[channels]
    grid = (sums[:channels] / jnp.maximum(counts, 1.0)[None, :]).astype(jnp.bfloat16)
    occupied = (counts > 0).astype(jnp.float32)

    full = lax.all_gather(grid, "chan", axis=0, tiled=True)
    masked = (grad_out.astype(jnp.float32) * occupied[None, :]).astype(jnp.bfloat16)

    stacked_w = weight.transpose(1, 0, 2).reshape(27 * out_rows, C_IN)
    wide = jnp.pad(full, ((0, 0), (REACH, REACH)))
    partial = jnp.dot(stacked_w, wide, preferred_element_type=jnp.float32)
    output = None
    for k in range(27):
        part = shifted(partial[k * out_rows : (k + 1) * out_rows], k, 1)
        output = part if output is None else output + part
    features_out = (output * occupied[None, :]).astype(jnp.bfloat16)

    moved = moved_stack(masked)
    grads = lax.dot_general(
        moved, full, (((1,), (1,)), ((), ())), preferred_element_type=jnp.float32
    )
    width = 27 * C_IN // tiles
    grads = grads.reshape(27, out_rows, C_IN).transpose(1, 0, 2).reshape(out_rows, tiles, width)
    chunks = grads.transpose(1, 0, 2).reshape(tiles, out_rows * width)
    arrived = lax.all_to_all(chunks, TILE_AXES, split_axis=0, concat_axis=0, tiled=True)
    weight_grad = jnp.sum(arrived, axis=0).reshape(out_rows, width)
    return (features_out, weight_grad)


def solution(mesh):
    tiles, chans = mesh.devices.shape
    split = Mesh(mesh.devices.reshape(4, tiles // 8, 2, chans), (*TILE_AXES, "chan"))
    tile = TILE_AXES
    placed = (
        P("chan", tile),
        P(tile, None),
        P(tile, None),
        P("chan", None, None),
        P("chan", tile),
    )

    def step(*args):
        return on_device(tiles, *args)

    return jax.shard_map(
        step,
        mesh=split,
        in_specs=placed,
        out_specs=(P("chan", tile), P("chan", tile)),
        check_vma=False,
    )
```

```python
import jax
import jax.numpy as jnp
import numpy as np
from jax import lax
from jax.sharding import Mesh
from jax.sharding import PartitionSpec as P

C_IN = 128
EDGE = 16
DEPTH = 8
VOX = 2048
OFFSETS = [(k // 9 - 1, k // 3 % 3 - 1, k % 3 - 1) for k in range(27)]
TILE_AXES = ("tx", "ty", "tc")


REACH = 256 + 16 + 1


def valid(a, b, e):
    v = lax.broadcasted_iota(jnp.int32, (1, VOX), 1)
    i, j, l = v // (EDGE * EDGE), v // EDGE % EDGE, v % EDGE
    return (
        (i + a >= 0) & (i + a < DEPTH) & (j + b >= 0) & (j + b < EDGE) & (l + e >= 0) & (l + e < EDGE)
    )


def shifted(padded, k, signs):
    a, b, e = (signs * x for x in OFFSETS[k])
    d = (a * EDGE + b) * EDGE + e
    part = padded[:, REACH + d : REACH + d + VOX]
    return jnp.where(valid(a, b, e), part, jnp.zeros_like(part))


def moved_stack(masked):
    v = lax.broadcasted_iota(jnp.int32, (1, VOX), 1)
    coords = (v // (EDGE * EDGE), v // EDGE % EDGE, v % EDGE)
    sizes = (DEPTH, EDGE, EDGE)
    strides = (EDGE * EDGE, EDGE, 1)
    stage = masked
    for axis in (2, 1, 0):
        step, size, where_ = strides[axis], sizes[axis], coords[axis]
        pads = [(0, 0)] * (stage.ndim - 1) + [(step, step)]
        wide = jnp.pad(stage, pads)
        parts = []
        for shift in (-1, 0, 1):
            part = wide[..., step - shift * step : step - shift * step + VOX]
            keep = (where_ - shift >= 0) & (where_ - shift < size)
            parts.append(jnp.where(keep, part, jnp.zeros_like(part)))
        stage = jnp.stack(parts)
    return stage.reshape(27 * masked.shape[0], VOX)


def on_device(tiles, points, dest, voxel, weight, grad_out):
    count = dest.shape[0]
    capacity = min(count, 3 * count // tiles)
    slots = tiles * capacity
    out_rows = weight.shape[0]
    channels = points.shape[0]

    onehot = (dest == jnp.arange(tiles, dtype=jnp.int32)[None, :]).astype(jnp.bfloat16)
    rows = jnp.arange(count, dtype=jnp.int32)
    earlier = (rows[:, None] > rows[None, :]).astype(jnp.bfloat16)
    before = jnp.dot(earlier, onehot, preferred_element_type=jnp.float32)
    rank = jnp.sum(before * onehot.astype(jnp.float32), axis=1).astype(jnp.int32)
    place = dest[:, 0] * capacity + rank

    vox = voxel[:, 0]
    codes = jnp.stack([vox // 64 + 1, vox % 64]).astype(jnp.bfloat16)
    payload = jnp.concatenate([points, codes], axis=0)
    select = (place[:, None] == jnp.arange(slots, dtype=jnp.int32)[None, :]).astype(jnp.bfloat16)
    send = jnp.dot(payload, select, preferred_element_type=jnp.float32).astype(jnp.bfloat16)
    received = lax.all_to_all(send, TILE_AXES, split_axis=1, concat_axis=1, tiled=True)

    high = received[channels].astype(jnp.int32)
    low = received[channels + 1].astype(jnp.int32)
    cell = jnp.where(high > 0, (high - 1) * 64 + low, VOX)
    member = (cell[:, None] == jnp.arange(VOX, dtype=jnp.int32)[None, :]).astype(jnp.bfloat16)
    summed = jnp.concatenate(
        [received[:channels], jnp.ones((1, slots), jnp.bfloat16)], axis=0
    )
    sums = jnp.dot(summed, member, preferred_element_type=jnp.float32)
    counts = sums[channels]
    grid = (sums[:channels] / jnp.maximum(counts, 1.0)[None, :]).astype(jnp.bfloat16)
    occupied = (counts > 0).astype(jnp.float32)

    full = lax.all_gather(grid, "chan", axis=0, tiled=True)
    masked = (grad_out.astype(jnp.float32) * occupied[None, :]).astype(jnp.bfloat16)

    stacked_w = weight.transpose(1, 0, 2).reshape(27 * out_rows, C_IN)
    wide = jnp.pad(full, ((0, 0), (REACH, REACH)))
    partial = jnp.dot(stacked_w, wide, preferred_element_type=jnp.float32)
    output = None
    for k in range(27):
        part = shifted(partial[k * out_rows : (k + 1) * out_rows], k, 1)
        output = part if output is None else output + part
    features_out = (output * occupied[None, :]).astype(jnp.bfloat16)

    moved = moved_stack(masked)
    grads = lax.dot_general(
        moved, full, (((1,), (1,)), ((), ())), preferred_element_type=jnp.float32
    )
    width = 27 * C_IN // tiles
    grads = grads.reshape(27, out_rows, C_IN).transpose(1, 0, 2).reshape(out_rows, tiles, width)
    lanes = -(-width // 128) * 128
    chunks = jnp.pad(grads, ((0, 0), (0, 0), (0, lanes - width))).transpose(1, 0, 2)
    arrived = lax.all_to_all(chunks, TILE_AXES, split_axis=0, concat_axis=0, tiled=True)
    weight_grad = jnp.sum(arrived, axis=0)[:, :width]
    return (features_out, weight_grad)


def solution(mesh):
    tiles, chans = mesh.devices.shape
    split = Mesh(mesh.devices.reshape(4, tiles // 8, 2, chans), (*TILE_AXES, "chan"))
    tile = TILE_AXES
    placed = (
        P("chan", tile),
        P(tile, None),
        P(tile, None),
        P("chan", None, None),
        P("chan", tile),
    )

    def step(*args):
        return on_device(tiles, *args)

    return jax.shard_map(
        step,
        mesh=split,
        in_specs=placed,
        out_specs=(P("chan", tile), P("chan", tile)),
        check_vma=False,
    )
```

```python
import jax
import jax.numpy as jnp
import numpy as np
from jax import lax
from jax.sharding import Mesh
from jax.sharding import PartitionSpec as P

C_IN = 128
EDGE = 16
DEPTH = 8
VOX = 2048
OFFSETS = [(k // 9 - 1, k // 3 % 3 - 1, k % 3 - 1) for k in range(27)]
TILE_AXES = ("tx", "ty", "tc")


REACH = 256 + 16 + 1


def valid(a, b, e):
    v = lax.broadcasted_iota(jnp.int32, (1, VOX), 1)
    i, j, l = v // (EDGE * EDGE), v // EDGE % EDGE, v % EDGE
    return (
        (i + a >= 0) & (i + a < DEPTH) & (j + b >= 0) & (j + b < EDGE) & (l + e >= 0) & (l + e < EDGE)
    )


def shifted(padded, k, signs):
    a, b, e = (signs * x for x in OFFSETS[k])
    d = (a * EDGE + b) * EDGE + e
    part = padded[:, REACH + d : REACH + d + VOX]
    return jnp.where(valid(a, b, e), part, jnp.zeros_like(part))


def moved_stack(masked):
    v = lax.broadcasted_iota(jnp.int32, (1, VOX), 1)
    coords = (v // (EDGE * EDGE), v // EDGE % EDGE, v % EDGE)
    sizes = (DEPTH, EDGE, EDGE)
    strides = (EDGE * EDGE, EDGE, 1)
    stage = masked
    for axis in (2, 1, 0):
        step, size, where_ = strides[axis], sizes[axis], coords[axis]
        pads = [(0, 0)] * (stage.ndim - 1) + [(step, step)]
        wide = jnp.pad(stage, pads)
        parts = []
        for shift in (-1, 0, 1):
            part = wide[..., step - shift * step : step - shift * step + VOX]
            keep = (where_ - shift >= 0) & (where_ - shift < size)
            parts.append(jnp.where(keep, part, jnp.zeros_like(part)))
        stage = jnp.stack(parts)
    return stage.reshape(27 * masked.shape[0], VOX)


def on_device(tiles, points, dest, voxel, weight, grad_out):
    count = dest.shape[0]
    capacity = min(count, 3 * count // tiles)
    slots = tiles * capacity
    out_rows = weight.shape[0]
    channels = points.shape[0]

    onehot = (dest == jnp.arange(tiles, dtype=jnp.int32)[None, :]).astype(jnp.bfloat16)
    rows = jnp.arange(count, dtype=jnp.int32)
    earlier = (rows[:, None] > rows[None, :]).astype(jnp.bfloat16)
    before = jnp.dot(earlier, onehot, preferred_element_type=jnp.float32)
    rank = jnp.sum(before * onehot.astype(jnp.float32), axis=1).astype(jnp.int32)
    place = dest[:, 0] * capacity + rank

    vox = voxel[:, 0]
    codes = jnp.stack([vox // 64 + 1, vox % 64]).astype(jnp.bfloat16)
    payload = jnp.concatenate([points, codes], axis=0)
    select = (place[:, None] == jnp.arange(slots, dtype=jnp.int32)[None, :]).astype(jnp.bfloat16)
    send = jnp.dot(payload, select, preferred_element_type=jnp.float32).astype(jnp.bfloat16)
    received = lax.all_to_all(send, TILE_AXES, split_axis=1, concat_axis=1, tiled=True)

    high = received[channels].astype(jnp.int32)
    low = received[channels + 1].astype(jnp.int32)
    cell = jnp.where(high > 0, (high - 1) * 64 + low, VOX)
    member = (cell[:, None] == jnp.arange(VOX, dtype=jnp.int32)[None, :]).astype(jnp.bfloat16)
    summed = jnp.concatenate(
        [received[:channels], jnp.ones((1, slots), jnp.bfloat16)], axis=0
    )
    sums = jnp.dot(summed, member, preferred_element_type=jnp.float32)
    counts = sums[channels]
    grid = (sums[:channels] / jnp.maximum(counts, 1.0)[None, :]).astype(jnp.bfloat16)
    occupied = (counts > 0).astype(jnp.float32)

    full = lax.all_gather(grid, "chan", axis=0, tiled=True)
    masked = (grad_out.astype(jnp.float32) * occupied[None, :]).astype(jnp.bfloat16)

    stacked_w = weight.transpose(1, 0, 2).reshape(27 * out_rows, C_IN)
    wide = jnp.pad(full, ((0, 0), (REACH, REACH)))
    partial = jnp.dot(stacked_w, wide, preferred_element_type=jnp.float32)
    output = None
    for k in range(27):
        part = shifted(partial[k * out_rows : (k + 1) * out_rows], k, 1)
        output = part if output is None else output + part
    features_out = (output * occupied[None, :]).astype(jnp.bfloat16)

    moved = moved_stack(masked)
    grads = lax.dot_general(
        moved, full, (((1,), (1,)), ((), ())), preferred_element_type=jnp.float32
    )
    width = 27 * C_IN // tiles
    grads = grads.reshape(27, out_rows, C_IN).transpose(1, 0, 2).reshape(out_rows, tiles, width)
    chunks = grads.transpose(1, 0, 2).reshape(tiles, 8, out_rows * width // 8)
    arrived = lax.all_to_all(chunks, TILE_AXES, split_axis=0, concat_axis=0, tiled=True)
    weight_grad = jnp.sum(arrived, axis=0).reshape(out_rows, width)
    return (features_out, weight_grad)


def solution(mesh):
    tiles, chans = mesh.devices.shape
    split = Mesh(mesh.devices.reshape(4, tiles // 8, 2, chans), (*TILE_AXES, "chan"))
    tile = TILE_AXES
    placed = (
        P("chan", tile),
        P(tile, None),
        P(tile, None),
        P("chan", None, None),
        P("chan", tile),
    )

    def step(*args):
        return on_device(tiles, *args)

    return jax.shard_map(
        step,
        mesh=split,
        in_specs=placed,
        out_specs=(P("chan", tile), P("chan", tile)),
        check_vma=False,
    )
```

```python
import jax
import jax.numpy as jnp
import numpy as np
from jax import lax
from jax.sharding import Mesh
from jax.sharding import PartitionSpec as P

C_IN = 128
EDGE = 16
DEPTH = 8
VOX = 2048
OFFSETS = [(k // 9 - 1, k // 3 % 3 - 1, k % 3 - 1) for k in range(27)]
TILE_AXES = ("tx", "ty", "tc")


REACH = 256 + 16 + 1


def valid(a, b, e):
    v = lax.broadcasted_iota(jnp.int32, (1, VOX), 1)
    i, j, l = v // (EDGE * EDGE), v // EDGE % EDGE, v % EDGE
    return (
        (i + a >= 0) & (i + a < DEPTH) & (j + b >= 0) & (j + b < EDGE) & (l + e >= 0) & (l + e < EDGE)
    )


def shifted(padded, k, signs):
    a, b, e = (signs * x for x in OFFSETS[k])
    d = (a * EDGE + b) * EDGE + e
    part = padded[:, REACH + d : REACH + d + VOX]
    return jnp.where(valid(a, b, e), part, jnp.zeros_like(part))


def moved_stack(masked):
    v = lax.broadcasted_iota(jnp.int32, (1, VOX), 1)
    coords = (v // (EDGE * EDGE), v // EDGE % EDGE, v % EDGE)
    sizes = (DEPTH, EDGE, EDGE)
    strides = (EDGE * EDGE, EDGE, 1)
    stage = masked
    for axis in (2, 1, 0):
        step, size, where_ = strides[axis], sizes[axis], coords[axis]
        pads = [(0, 0)] * (stage.ndim - 1) + [(step, step)]
        wide = jnp.pad(stage, pads)
        parts = []
        for shift in (-1, 0, 1):
            part = wide[..., step - shift * step : step - shift * step + VOX]
            keep = (where_ - shift >= 0) & (where_ - shift < size)
            parts.append(jnp.where(keep, part, jnp.zeros_like(part)))
        stage = jnp.stack(parts)
    return stage.reshape(27 * masked.shape[0], VOX)


def on_device(tiles, points, dest, voxel, weight, grad_out):
    count = dest.shape[0]
    capacity = min(count, 3 * count // tiles)
    slots = tiles * capacity
    out_rows = weight.shape[0]
    channels = points.shape[0]

    onehot = (dest == jnp.arange(tiles, dtype=jnp.int32)[None, :]).astype(jnp.bfloat16)
    block = 128 if count % 128 == 0 else count
    blocks = count // block
    rows = jnp.arange(block, dtype=jnp.int32)
    earlier = (rows[:, None] > rows[None, :]).astype(jnp.bfloat16)
    grouped = onehot.reshape(blocks, block, tiles)
    within = jnp.einsum("ij,bjt->bit", earlier, grouped, preferred_element_type=jnp.float32)
    ahead = jnp.arange(blocks, dtype=jnp.int32)
    prior = (ahead[:, None] > ahead[None, :]).astype(jnp.float32)
    totals = jnp.sum(grouped.astype(jnp.float32), axis=1)
    offset = jnp.dot(prior, totals, precision=lax.Precision.HIGHEST)
    before = (within + offset[:, None, :]).reshape(count, tiles)
    rank = jnp.sum(before * onehot.astype(jnp.float32), axis=1).astype(jnp.int32)
    place = dest[:, 0] * capacity + rank

    vox = voxel[:, 0]
    codes = jnp.stack([vox // 64 + 1, vox % 64]).astype(jnp.bfloat16)
    payload = jnp.concatenate([points, codes], axis=0)
    select = (place[:, None] == jnp.arange(slots, dtype=jnp.int32)[None, :]).astype(jnp.bfloat16)
    send = jnp.dot(payload, select, preferred_element_type=jnp.float32).astype(jnp.bfloat16)
    received = lax.all_to_all(send, TILE_AXES, split_axis=1, concat_axis=1, tiled=True)

    high = received[channels].astype(jnp.int32)
    low = received[channels + 1].astype(jnp.int32)
    cell = jnp.where(high > 0, (high - 1) * 64 + low, VOX)
    member = (cell[:, None] == jnp.arange(VOX, dtype=jnp.int32)[None, :]).astype(jnp.bfloat16)
    summed = jnp.concatenate(
        [received[:channels], jnp.ones((1, slots), jnp.bfloat16)], axis=0
    )
    sums = jnp.dot(summed, member, preferred_element_type=jnp.float32)
    counts = sums[channels]
    grid = (sums[:channels] / jnp.maximum(counts, 1.0)[None, :]).astype(jnp.bfloat16)
    occupied = (counts > 0).astype(jnp.float32)

    full = lax.all_gather(grid, "chan", axis=0, tiled=True)
    masked = (grad_out.astype(jnp.float32) * occupied[None, :]).astype(jnp.bfloat16)

    stacked_w = weight.transpose(1, 0, 2).reshape(27 * out_rows, C_IN)
    wide = jnp.pad(full, ((0, 0), (REACH, REACH)))
    partial = jnp.dot(stacked_w, wide, preferred_element_type=jnp.float32)
    output = None
    for k in range(27):
        part = shifted(partial[k * out_rows : (k + 1) * out_rows], k, 1)
        output = part if output is None else output + part
    features_out = (output * occupied[None, :]).astype(jnp.bfloat16)

    moved = moved_stack(masked)
    grads = lax.dot_general(
        moved, full, (((1,), (1,)), ((), ())), preferred_element_type=jnp.float32
    )
    width = 27 * C_IN // tiles
    grads = grads.reshape(27, out_rows, C_IN).transpose(1, 0, 2).reshape(out_rows, tiles, width)
    chunks = grads.transpose(1, 0, 2).reshape(tiles, 8, out_rows * width // 8)
    arrived = lax.all_to_all(chunks, TILE_AXES, split_axis=0, concat_axis=0, tiled=True)
    weight_grad = jnp.sum(arrived, axis=0).reshape(out_rows, width)
    return (features_out, weight_grad)


def solution(mesh):
    tiles, chans = mesh.devices.shape
    split = Mesh(mesh.devices.reshape(4, tiles // 8, 2, chans), (*TILE_AXES, "chan"))
    tile = TILE_AXES
    placed = (
        P("chan", tile),
        P(tile, None),
        P(tile, None),
        P("chan", None, None),
        P("chan", tile),
    )

    def step(*args):
        return on_device(tiles, *args)

    return jax.shard_map(
        step,
        mesh=split,
        in_specs=placed,
        out_specs=(P("chan", tile), P("chan", tile)),
        check_vma=False,
    )
```

```python
import jax
import jax.numpy as jnp
import numpy as np
from jax import lax
from jax.sharding import Mesh
from jax.sharding import PartitionSpec as P

C_IN = 128
EDGE = 16
DEPTH = 8
VOX = 2048
OFFSETS = [(k // 9 - 1, k // 3 % 3 - 1, k % 3 - 1) for k in range(27)]
TILE_AXES = ("tx", "ty", "tc")


REACH = 256 + 16 + 1


def valid(a, b, e):
    v = lax.broadcasted_iota(jnp.int32, (1, VOX), 1)
    i, j, l = v // (EDGE * EDGE), v // EDGE % EDGE, v % EDGE
    return (
        (i + a >= 0) & (i + a < DEPTH) & (j + b >= 0) & (j + b < EDGE) & (l + e >= 0) & (l + e < EDGE)
    )


def shifted(padded, k, signs):
    a, b, e = (signs * x for x in OFFSETS[k])
    d = (a * EDGE + b) * EDGE + e
    part = padded[:, REACH + d : REACH + d + VOX]
    return jnp.where(valid(a, b, e), part, jnp.zeros_like(part))


def moved_stack(masked):
    v = lax.broadcasted_iota(jnp.int32, (1, VOX), 1)
    coords = (v // (EDGE * EDGE), v // EDGE % EDGE, v % EDGE)
    sizes = (DEPTH, EDGE, EDGE)
    strides = (EDGE * EDGE, EDGE, 1)
    stage = masked
    for axis in (2, 1, 0):
        step, size, where_ = strides[axis], sizes[axis], coords[axis]
        pads = [(0, 0)] * (stage.ndim - 1) + [(step, step)]
        wide = jnp.pad(stage, pads)
        parts = []
        for shift in (-1, 0, 1):
            part = wide[..., step - shift * step : step - shift * step + VOX]
            keep = (where_ - shift >= 0) & (where_ - shift < size)
            parts.append(jnp.where(keep, part, jnp.zeros_like(part)))
        stage = jnp.stack(parts)
    return stage.reshape(27 * masked.shape[0], VOX)


def on_device(tiles, points, dest, voxel, weight, grad_out):
    count = dest.shape[0]
    capacity = min(count, 3 * count // tiles)
    slots = tiles * capacity
    out_rows = weight.shape[0]
    channels = points.shape[0]

    onehot = (dest == jnp.arange(tiles, dtype=jnp.int32)[None, :]).astype(jnp.bfloat16)
    rows = jnp.arange(count, dtype=jnp.int32)
    earlier = (rows[:, None] > rows[None, :]).astype(jnp.bfloat16)
    before = jnp.dot(earlier, onehot, preferred_element_type=jnp.float32)
    rank = jnp.sum(before * onehot.astype(jnp.float32), axis=1).astype(jnp.int32)
    place = dest[:, 0] * capacity + rank

    vox = voxel[:, 0]
    codes = jnp.stack([vox // 64 + 1, vox % 64]).astype(jnp.bfloat16)
    payload = jnp.concatenate([points, codes], axis=0)
    select = (place[:, None] == jnp.arange(slots, dtype=jnp.int32)[None, :]).astype(jnp.bfloat16)
    send = jnp.dot(payload, select, preferred_element_type=jnp.float32).astype(jnp.bfloat16)
    received = lax.all_to_all(send, TILE_AXES, split_axis=1, concat_axis=1, tiled=True)

    high = received[channels].astype(jnp.int32)
    low = received[channels + 1].astype(jnp.int32)
    upper = (high[:, None] - 1 == jnp.arange(VOX // 64, dtype=jnp.int32)[None, :]).astype(jnp.bfloat16)
    lower = low[None, :] == jnp.arange(64, dtype=jnp.int32)[:, None]
    summed = jnp.concatenate(
        [received[:channels], jnp.ones((1, slots), jnp.bfloat16)], axis=0
    )
    spread = jnp.where(lower[None], summed[:, None, :], jnp.zeros((), jnp.bfloat16))
    split = jnp.dot(spread.reshape((channels + 1) * 64, slots), upper, preferred_element_type=jnp.float32)
    sums = split.reshape(channels + 1, 64, VOX // 64).transpose(0, 2, 1).reshape(channels + 1, VOX)
    counts = sums[channels]
    grid = (sums[:channels] / jnp.maximum(counts, 1.0)[None, :]).astype(jnp.bfloat16)
    occupied = (counts > 0).astype(jnp.float32)

    full = lax.all_gather(grid, "chan", axis=0, tiled=True)
    masked = (grad_out.astype(jnp.float32) * occupied[None, :]).astype(jnp.bfloat16)

    stacked_w = weight.transpose(1, 0, 2).reshape(27 * out_rows, C_IN)
    wide = jnp.pad(full, ((0, 0), (REACH, REACH)))
    partial = jnp.dot(stacked_w, wide, preferred_element_type=jnp.float32)
    output = None
    for k in range(27):
        part = shifted(partial[k * out_rows : (k + 1) * out_rows], k, 1)
        output = part if output is None else output + part
    features_out = (output * occupied[None, :]).astype(jnp.bfloat16)

    moved = moved_stack(masked)
    grads = lax.dot_general(
        moved, full, (((1,), (1,)), ((), ())), preferred_element_type=jnp.float32
    )
    width = 27 * C_IN // tiles
    grads = grads.reshape(27, out_rows, C_IN).transpose(1, 0, 2).reshape(out_rows, tiles, width)
    chunks = grads.transpose(1, 0, 2).reshape(tiles, 8, out_rows * width // 8)
    arrived = lax.all_to_all(chunks, TILE_AXES, split_axis=0, concat_axis=0, tiled=True)
    weight_grad = jnp.sum(arrived, axis=0).reshape(out_rows, width)
    return (features_out, weight_grad)


def solution(mesh):
    tiles, chans = mesh.devices.shape
    split = Mesh(mesh.devices.reshape(4, tiles // 8, 2, chans), (*TILE_AXES, "chan"))
    tile = TILE_AXES
    placed = (
        P("chan", tile),
        P(tile, None),
        P(tile, None),
        P("chan", None, None),
        P("chan", tile),
    )

    def step(*args):
        return on_device(tiles, *args)

    return jax.shard_map(
        step,
        mesh=split,
        in_specs=placed,
        out_specs=(P("chan", tile), P("chan", tile)),
        check_vma=False,
    )
```

```python
import jax
import jax.numpy as jnp
import numpy as np
from jax import lax
from jax.sharding import Mesh
from jax.sharding import PartitionSpec as P

C_IN = 128
EDGE = 16
DEPTH = 8
VOX = 2048
OFFSETS = [(k // 9 - 1, k // 3 % 3 - 1, k % 3 - 1) for k in range(27)]
TILE_AXES = ("tx", "ty", "tc")


REACH = 256 + 16 + 1


def valid(a, b, e):
    v = lax.broadcasted_iota(jnp.int32, (1, VOX), 1)
    i, j, l = v // (EDGE * EDGE), v // EDGE % EDGE, v % EDGE
    return (
        (i + a >= 0) & (i + a < DEPTH) & (j + b >= 0) & (j + b < EDGE) & (l + e >= 0) & (l + e < EDGE)
    )


def shifted(padded, k, signs):
    a, b, e = (signs * x for x in OFFSETS[k])
    d = (a * EDGE + b) * EDGE + e
    part = padded[:, REACH + d : REACH + d + VOX]
    return jnp.where(valid(a, b, e), part, jnp.zeros_like(part))


def moved_stack(masked):
    v = lax.broadcasted_iota(jnp.int32, (1, VOX), 1)
    coords = (v // (EDGE * EDGE), v // EDGE % EDGE, v % EDGE)
    sizes = (DEPTH, EDGE, EDGE)
    strides = (EDGE * EDGE, EDGE, 1)
    stage = masked
    for axis in (2, 1, 0):
        step, size, where_ = strides[axis], sizes[axis], coords[axis]
        pads = [(0, 0)] * (stage.ndim - 1) + [(step, step)]
        wide = jnp.pad(stage, pads)
        parts = []
        for shift in (-1, 0, 1):
            part = wide[..., step - shift * step : step - shift * step + VOX]
            keep = (where_ - shift >= 0) & (where_ - shift < size)
            parts.append(jnp.where(keep, part, jnp.zeros_like(part)))
        stage = jnp.stack(parts)
    return stage.reshape(27 * masked.shape[0], VOX)


def on_device(tiles, points, dest, voxel, weight, grad_out):
    count = dest.shape[0]
    capacity = min(count, 3 * count // tiles)
    slots = tiles * capacity
    out_rows = weight.shape[0]
    channels = points.shape[0]

    onehot = (dest == jnp.arange(tiles, dtype=jnp.int32)[None, :]).astype(jnp.bfloat16)
    rows = jnp.arange(count, dtype=jnp.int32)
    earlier = (rows[:, None] > rows[None, :]).astype(jnp.bfloat16)
    before = jnp.dot(earlier, onehot, preferred_element_type=jnp.float32)
    rank = jnp.sum(before * onehot.astype(jnp.float32), axis=1).astype(jnp.int32)
    place = dest[:, 0] * capacity + rank

    vox = voxel[:, 0]
    codes = jnp.stack([vox // 64 + 1, vox % 64]).astype(jnp.bfloat16)
    payload = jnp.concatenate([points, codes], axis=0)
    rows_in = payload.shape[0]
    ranked = rank[None, :] == jnp.arange(capacity, dtype=jnp.int32)[:, None]
    spread_in = jnp.where(ranked[None], payload[:, None, :], jnp.zeros((), jnp.bfloat16))
    packed = jnp.dot(spread_in.reshape(rows_in * capacity, count), onehot, preferred_element_type=jnp.float32)
    send = packed.astype(jnp.bfloat16).reshape(rows_in, capacity, tiles).transpose(0, 2, 1).reshape(rows_in, slots)
    received = lax.all_to_all(send, TILE_AXES, split_axis=1, concat_axis=1, tiled=True)

    high = received[channels].astype(jnp.int32)
    low = received[channels + 1].astype(jnp.int32)
    upper = (high[:, None] - 1 == jnp.arange(VOX // 64, dtype=jnp.int32)[None, :]).astype(jnp.bfloat16)
    lower = low[None, :] == jnp.arange(64, dtype=jnp.int32)[:, None]
    summed = jnp.concatenate(
        [received[:channels], jnp.ones((1, slots), jnp.bfloat16)], axis=0
    )
    spread = jnp.where(lower[None], summed[:, None, :], jnp.zeros((), jnp.bfloat16))
    split = jnp.dot(spread.reshape((channels + 1) * 64, slots), upper, preferred_element_type=jnp.float32)
    sums = split.reshape(channels + 1, 64, VOX // 64).transpose(0, 2, 1).reshape(channels + 1, VOX)
    counts = sums[channels]
    grid = (sums[:channels] / jnp.maximum(counts, 1.0)[None, :]).astype(jnp.bfloat16)
    occupied = (counts > 0).astype(jnp.float32)

    full = lax.all_gather(grid, "chan", axis=0, tiled=True)
    masked = (grad_out.astype(jnp.float32) * occupied[None, :]).astype(jnp.bfloat16)

    stacked_w = weight.transpose(1, 0, 2).reshape(27 * out_rows, C_IN)
    wide = jnp.pad(full, ((0, 0), (REACH, REACH)))
    partial = jnp.dot(stacked_w, wide, preferred_element_type=jnp.float32)
    output = None
    for k in range(27):
        part = shifted(partial[k * out_rows : (k + 1) * out_rows], k, 1)
        output = part if output is None else output + part
    features_out = (output * occupied[None, :]).astype(jnp.bfloat16)

    moved = moved_stack(masked)
    grads = lax.dot_general(
        moved, full, (((1,), (1,)), ((), ())), preferred_element_type=jnp.float32
    )
    width = 27 * C_IN // tiles
    grads = grads.reshape(27, out_rows, C_IN).transpose(1, 0, 2).reshape(out_rows, tiles, width)
    chunks = grads.transpose(1, 0, 2).reshape(tiles, 8, out_rows * width // 8)
    arrived = lax.all_to_all(chunks, TILE_AXES, split_axis=0, concat_axis=0, tiled=True)
    weight_grad = jnp.sum(arrived, axis=0).reshape(out_rows, width)
    return (features_out, weight_grad)


def solution(mesh):
    tiles, chans = mesh.devices.shape
    split = Mesh(mesh.devices.reshape(4, tiles // 8, 2, chans), (*TILE_AXES, "chan"))
    tile = TILE_AXES
    placed = (
        P("chan", tile),
        P(tile, None),
        P(tile, None),
        P("chan", None, None),
        P("chan", tile),
    )

    def step(*args):
        return on_device(tiles, *args)

    return jax.shard_map(
        step,
        mesh=split,
        in_specs=placed,
        out_specs=(P("chan", tile), P("chan", tile)),
        check_vma=False,
    )
```
